512 devices in a mesh: dp: 64 (over x, z, y_lo), tensor: 8 (over y_hi, core).
Axes of the slice: x: 4, y: 8 (y_hi: 4, y_lo: 2; y = y_hi * 2 + y_lo), z: 8, core: 2. Of those that a mesh axis runs over, the one named last changes fastest.
Arguments:
- tokens: bfloat16 [16384, 8192], P('dp', 'tensor'), may hold values from -6 to 6
- norm_gain: bfloat16 [8192], P('tensor'), may hold values from 0.099609375 to 1.8984375
- kept_blocks: bfloat16 [8192, 6144], P('dp', 'tensor'), may hold values from -0.09375 to 0.09375
- block_cols: int32 [64, 48], P('dp', 'tensor'), may hold values from 0 to 9, as said below
- row_counts: int32 [64, 8], P('dp', 'tensor'), may hold values from 4 to 6, as said below
Outputs:
- projected: bfloat16 [16384, 10240], P('dp', 'tensor')
The draws below stay inside these ranges and needn't reach their ends.
Inputs may be any that keep to these rules, and one draw needn't show every extreme that they name: `block_cols`: in each row block the 6 slots of one shard name distinct column blocks of that shard, also the slots beyond row_counts. `row_counts`: in every shard some row block has 6 kept blocks.
All inputs are finite; a program needn't handle non-finite values.
Results may differ from the reference program's by a relative error of at most 0.0049.
Values may be sent and summed in bfloat16 or wider, within the bound.
No kernel may reach another device: no remote copies, remote signals or barrier semaphores. Data moves between devices by JAX's collectives and lax.ppermute only.
A program may use at most 128 MiB of HBM per device.

```python
import jax
import jax.numpy as jnp
from jax import lax

D = 8192
GROUP = 8
HD = 128
BS = 128
TOK_DEV = 256
TOKENS = 16384
SHARDS = 8
QKV = 10240
BLK_DEV = 10
LOW = 4
CAP = 6
SLOTS = 48
RB = 64


def shared_layout(key):
    count_key, fullest_key, order_key = jax.random.split(key, 3)
    counts = jax.random.randint(count_key, (RB, SHARDS), LOW, CAP + 1)
    fullest = jax.random.randint(fullest_key, (SHARDS,), 0, RB)
    counts = jnp.where(jnp.arange(RB)[:, None] == fullest[None, :], CAP, counts)
    scores = jax.random.randint(order_key, (RB, SHARDS, BLK_DEV), 0, 1 << 20) * BLK_DEV + jnp.arange(BLK_DEV)[None, None, :]
    ranking = jnp.argsort(scores, axis=-1)
    columns = ranking[:, :, :CAP].reshape(RB, SHARDS * CAP)
    return (counts.astype(jnp.int32), columns.astype(jnp.int32))


def draw_block_cols(key, part):
    return shared_layout(jax.random.fold_in(key, 11))[1]


def draw_row_counts(key, part):
    return shared_layout(jax.random.fold_in(key, 11))[0]


def shard_levels(rng, extent, pieces, least, high):
    def one(axis_at, shards_of):
        draws = jax.random.uniform(jax.random.fold_in(jax.random.fold_in(rng, 6), axis_at), (shards_of,), jnp.float32, least / len(pieces), high / len(pieces))
        return jnp.repeat(jnp.exp(draws), extent[axis_at] // shards_of).reshape((-1,) + (1,) * (len(extent) - axis_at - 1))

    gain = one(*pieces[0])
    for cut in pieces[1:]:
        gain = gain * one(*cut)
    return gain


def normal_values(stream_key, shape, width, limit, pieces=(), kind=jnp.bfloat16):
    drawn = width * jax.random.normal(stream_key, shape, jnp.float32)
    if pieces:
        drawn = drawn * shard_levels(stream_key, shape, pieces, -0.22, 0.18)
    return jnp.clip(drawn, -limit, limit).astype(kind)


def setup_inputs(seed: int = 0) -> dict:
    key_of = jax.random.split(jax.random.key(seed), 6)
    return {
        "tokens": normal_values(key_of[0], (TOKENS, D), 1.0, 6.0, ((0, 64), (1, 8))),
        "norm_gain": jnp.clip(1.0 + 0.18 * jax.random.normal(key_of[1], (D,), jnp.float32), 0.099609375, 1.8984375).astype(jnp.bfloat16),
        "kept_blocks": normal_values(key_of[2], (D, SLOTS * BS), (D // 2) ** -0.5, 0.09375, ((0, 64), (1, 8))),
        "block_cols": draw_block_cols(jax.random.fold_in(key_of[5], 71), 0),
        "row_counts": draw_row_counts(jax.random.fold_in(key_of[5], 71), 0),
    }


rope_theta = 500000.0

def rotate(mixed, positions):
    row_count = mixed.shape[0]
    head_view = mixed.reshape(row_count, -1, GROUP + 2, HD)
    half_size = HD // 2
    inverse_freq = rope_theta ** (-(jnp.arange(half_size).astype(jnp.float32) * 2.0 / HD))
    angles = positions[:, None] * inverse_freq[None, :]
    cosine = jnp.cos(angles)[:, None, None, :]
    sine_part = jnp.sin(angles)[:, None, None, :]
    first_half = head_view[..., :half_size]
    second = head_view[..., half_size:]
    turned = jnp.concatenate([first_half * cosine - second * sine_part, second * cosine + first_half * sine_part], axis=-1)
    rotated_heads = (jnp.arange(GROUP + 2) < GROUP + 1)[None, None, :, None]
    return jnp.where(rotated_heads, turned, head_view).reshape(row_count, -1)

def reference(tokens, norm_gain, kept_blocks, block_cols, row_counts):
    shards = SLOTS // CAP
    floats = tokens.astype(jnp.float32)
    mean_square = lax.optimization_barrier(jnp.mean(floats * floats, axis=-1, keepdims=True))
    normed = (floats * lax.rsqrt(mean_square + 1e-05) * norm_gain.astype(jnp.float32)).astype(jnp.bfloat16)
    blocks = kept_blocks.reshape(RB, BS, shards, CAP, BS)
    columns = block_cols.reshape(RB, shards, CAP)
    filled = jnp.arange(CAP)[None, None, :] < row_counts[:, :, None]
    placing = ((columns[:, :, :, None] == jnp.arange(BLK_DEV)[None, None, None, :]) & filled[..., None]).astype(jnp.float32)
    positions = (jnp.arange(TOKENS) % TOK_DEV).astype(jnp.float32)

    def one_shard(shard_index):
        shard_blocks = lax.dynamic_index_in_dim(blocks, shard_index, 2, keepdims=False).astype(jnp.float32)
        shard_place = lax.dynamic_index_in_dim(placing, shard_index, 1, keepdims=False)
        dense_rows = jnp.einsum('rksj,rsc->rkcj', shard_blocks, shard_place).astype(jnp.bfloat16).reshape(D, BLK_DEV * BS)
        mixed = jnp.dot(normed, dense_rows, preferred_element_type=jnp.float32)
        return rotate(mixed, positions).astype(jnp.bfloat16)
    results = lax.map(one_shard, jnp.arange(shards))
    return jnp.transpose(results, (1, 0, 2)).reshape(TOKENS, QKV)
```

```python
import functools

import jax
import jax.numpy as jnp
from jax import lax
from jax.experimental import pallas as pl
from jax.experimental.pallas import tpu as pltpu
from jax.sharding import Mesh
from jax.sharding import PartitionSpec as P

KVH = 8
GROUP = 8
HD = 128
BS = 128
ROWS_PER_STEP = 8

rope_theta = 500000.0

DP = ("x", "z", "ylo")
TP = ("yhi", "core")


def rope_tables(count):
    half_size = HD // 2
    positions = jnp.arange(count).astype(jnp.float32)
    inverse_freq = rope_theta ** (-(jnp.arange(half_size).astype(jnp.float32) * 2.0 / HD))
    angles = positions[:, None] * inverse_freq[None, :]
    cosine = jnp.cos(angles)
    sine_part = jnp.sin(angles)
    return (
        jnp.concatenate([cosine, cosine], axis=1),
        jnp.concatenate([-sine_part, sine_part], axis=1),
    )


def qkv_kernel(heads, slots, steps, dest_ref, normed_ref, w_ref, cos_ref, sin_ref, out_ref, acc_ref):
    step = pl.program_id(0)

    @pl.when(step == 0)
    def _():
        acc_ref[...] = jnp.zeros_like(acc_ref)

    for j in range(ROWS_PER_STEP):
        row = step * ROWS_PER_STEP + j
        y = jnp.dot(
            normed_ref[:, j * BS:(j + 1) * BS],
            w_ref[j * BS:(j + 1) * BS, :],
            preferred_element_type=jnp.float32,
        )
        for s in range(slots):
            d = dest_ref[row * slots + s]
            acc_ref[d] += y[:, s * BS:(s + 1) * BS]

    @pl.when(step == steps - 1)
    def _():
        cos = cos_ref[...]
        sin = sin_ref[...]
        for c in range(heads):
            x = acc_ref[c]
            if c < GROUP + 1:
                x = x * cos + pltpu.roll(x, HD // 2, 1) * sin
            out_ref[:, c * BS:(c + 1) * BS] = x.astype(out_ref.dtype)


def block_sparse_qkv(dest, normed, w, cos, sin, heads, slots):
    tokens = normed.shape[0]
    feature_count = normed.shape[1]
    steps = feature_count // (ROWS_PER_STEP * BS)
    chunk = ROWS_PER_STEP * BS
    kernel = functools.partial(qkv_kernel, heads, slots, steps)
    flops = 2 * tokens * feature_count * slots * BS
    bytes_accessed = normed.size * 2 + w.size * 2 + tokens * heads * BS * 2
    return pl.pallas_call(
        kernel,
        out_shape=jax.ShapeDtypeStruct((tokens, heads * BS), jnp.bfloat16),
        grid_spec=pltpu.PrefetchScalarGridSpec(
            num_scalar_prefetch=1,
            grid=(steps,),
            in_specs=[
                pl.BlockSpec((tokens, chunk), lambda i, d: (0, i)),
                pl.BlockSpec((chunk, slots * BS), lambda i, d: (i, 0)),
                pl.BlockSpec((tokens, HD), lambda i, d: (0, 0)),
                pl.BlockSpec((tokens, HD), lambda i, d: (0, 0)),
            ],
            out_specs=pl.BlockSpec((tokens, heads * BS), lambda i, d: (0, 0)),
            scratch_shapes=[pltpu.VMEM((heads + 1, tokens, BS), jnp.float32)],
        ),
        compiler_params=pltpu.CompilerParams(dimension_semantics=("arbitrary",)),
        cost_estimate=pl.CostEstimate(flops=flops, bytes_accessed=bytes_accessed, transcendentals=0),
    )(dest, normed, w, cos, sin)


def per_device(tokens, norm_gain, kept_blocks, block_cols, row_counts):
    tensor_count = lax.axis_size(TP)
    heads = KVH // tensor_count * (GROUP + 2) * HD // BS
    slots = block_cols.shape[1]

    w = lax.all_gather(kept_blocks, "ylo", axis=0, tiled=True)
    w = lax.all_gather(w, ("x", "z"), axis=0, tiled=True)

    dest_here = jnp.where(jnp.arange(slots)[None, :] < row_counts, block_cols, heads)
    dest = lax.all_gather(dest_here, DP, axis=0, tiled=True).reshape(-1)

    gathered = lax.all_gather(tokens, TP, axis=1, tiled=True)
    gain_all = lax.all_gather(norm_gain, TP, axis=0, tiled=True)
    floats = gathered.astype(jnp.float32)
    mean_square = jnp.mean(floats * floats, axis=-1, keepdims=True)
    normed = (floats * lax.rsqrt(mean_square + 1e-05) * gain_all.astype(jnp.float32)).astype(
        jnp.bfloat16
    )
    cos, sin = rope_tables(tokens.shape[0])
    return block_sparse_qkv(dest, normed, w, cos, sin, heads, slots)


def solution(mesh):
    dp_size = mesh.shape["dp"]
    tp_size = mesh.shape["tensor"]
    fine = Mesh(mesh.devices.reshape(dp_size // 16, 8, 2, tp_size // 2, 2), DP + TP)
    spec = P(DP, TP)
    in_specs = (spec, P(TP), spec, spec, spec)
    return jax.shard_map(per_device, mesh=fine, in_specs=in_specs, out_specs=spec, check_vma=False)
```

```python
import functools

import jax
import jax.numpy as jnp
from jax import lax
from jax.experimental import pallas as pl
from jax.experimental.pallas import tpu as pltpu
from jax.sharding import Mesh
from jax.sharding import PartitionSpec as P

KVH = 8
GROUP = 8
HD = 128
BS = 128
ROWS_PER_STEP = 8

rope_theta = 500000.0

DP = ("x", "z", "ylo")
TP = ("yhi", "core")


def rotate(mixed, positions):
    row_count = mixed.shape[0]
    head_view = mixed.reshape(row_count, -1, GROUP + 2, HD)
    half_size = HD // 2
    inverse_freq = rope_theta ** (-(jnp.arange(half_size).astype(jnp.float32) * 2.0 / HD))
    angles = positions[:, None] * inverse_freq[None, :]
    cosine = jnp.cos(angles)[:, None, None, :]
    sine_part = jnp.sin(angles)[:, None, None, :]
    first_half = head_view[..., :half_size]
    second = head_view[..., half_size:]
    turned = jnp.concatenate(
        [first_half * cosine - second * sine_part, second * cosine + first_half * sine_part],
        axis=-1,
    )
    rotated_heads = (jnp.arange(GROUP + 2) < GROUP + 1)[None, None, :, None]
    return jnp.where(rotated_heads, turned, head_view).reshape(row_count, -1)


def partial_kernel(heads, slots, steps, dest_ref, x_ref, w_ref, out_ref, acc_ref):
    step = pl.program_id(0)

    @pl.when(step == 0)
    def _():
        acc_ref[...] = jnp.zeros_like(acc_ref)

    for j in range(ROWS_PER_STEP):
        row = step * ROWS_PER_STEP + j
        y = jnp.dot(
            x_ref[:, j * BS:(j + 1) * BS],
            w_ref[j * BS:(j + 1) * BS, :],
            preferred_element_type=jnp.float32,
        )
        for s in range(slots):
            d = dest_ref[row * slots + s]
            acc_ref[d] += y[:, s * BS:(s + 1) * BS]

    @pl.when(step == steps - 1)
    def _():
        for c in range(heads):
            out_ref[:, c * BS:(c + 1) * BS] = acc_ref[c]


def block_sparse_partial(dest, x, w, heads, slots):
    tokens, feature_count = x.shape
    steps = feature_count // (ROWS_PER_STEP * BS)
    chunk = ROWS_PER_STEP * BS
    kernel = functools.partial(partial_kernel, heads, slots, steps)
    flops = 2 * tokens * feature_count * slots * BS
    bytes_accessed = x.size * 2 + w.size * 2 + tokens * heads * BS * 4
    return pl.pallas_call(
        kernel,
        out_shape=jax.ShapeDtypeStruct((tokens, heads * BS), jnp.float32),
        grid_spec=pltpu.PrefetchScalarGridSpec(
            num_scalar_prefetch=1,
            grid=(steps,),
            in_specs=[
                pl.BlockSpec((tokens, chunk), lambda i, d: (0, i)),
                pl.BlockSpec((chunk, slots * BS), lambda i, d: (i, 0)),
            ],
            out_specs=pl.BlockSpec((tokens, heads * BS), lambda i, d: (0, 0)),
            scratch_shapes=[pltpu.VMEM((heads + 1, tokens, BS), jnp.float32)],
        ),
        compiler_params=pltpu.CompilerParams(dimension_semantics=("arbitrary",)),
        cost_estimate=pl.CostEstimate(flops=flops, bytes_accessed=bytes_accessed, transcendentals=0),
    )(dest, x, w)


def per_device(tokens, norm_gain, kept_blocks, block_cols, row_counts):
    tensor_count = lax.axis_size(TP)
    heads = KVH // tensor_count * (GROUP + 2) * HD // BS
    slots = block_cols.shape[1]
    pair = lax.axis_size("ylo")
    swap = [(i, (i + 1) % pair) for i in range(pair)]
    half = lax.axis_index("ylo")
    token_count = tokens.shape[0]

    w = lax.all_gather(kept_blocks, ("x", "z"), axis=0, tiled=True)
    dest_here = jnp.where(jnp.arange(slots)[None, :] < row_counts, block_cols, heads)
    dest = lax.all_gather(dest_here, ("x", "z"), axis=0, tiled=True).reshape(-1)

    gathered = lax.all_gather(tokens, TP, axis=1, tiled=True)
    gain_all = lax.all_gather(norm_gain, TP, axis=0, tiled=True)
    floats = gathered.astype(jnp.float32)
    mean_square = jnp.mean(floats * floats, axis=-1, keepdims=True)
    normed = (floats * lax.rsqrt(mean_square + 1e-05) * gain_all.astype(jnp.float32)).astype(
        jnp.bfloat16
    )
    by_half = normed.reshape(token_count, -1, pair, BS)
    mine = lax.dynamic_index_in_dim(by_half, half, 2, keepdims=False).reshape(token_count, -1)
    theirs = lax.dynamic_index_in_dim(by_half, 1 - half, 2, keepdims=False).reshape(token_count, -1)
    received = lax.ppermute(theirs, "ylo", swap)
    x = jnp.concatenate([mine, received], axis=0)

    partial = block_sparse_partial(dest, x, w, heads, slots)
    returned = lax.ppermute(partial[token_count:], "ylo", swap)
    mixed = partial[:token_count] + returned
    positions = jnp.arange(token_count).astype(jnp.float32)
    return rotate(mixed, positions).astype(jnp.bfloat16)


def solution(mesh):
    dp_size = mesh.shape["dp"]
    tp_size = mesh.shape["tensor"]
    fine = Mesh(mesh.devices.reshape(dp_size // 16, 8, 2, tp_size // 2, 2), DP + TP)
    spec = P(DP, TP)
    in_specs = (spec, P(TP), spec, spec, spec)
    return jax.shard_map(per_device, mesh=fine, in_specs=in_specs, out_specs=spec, check_vma=False)
```

```python
import functools

import jax
import jax.numpy as jnp
from jax import lax
from jax.experimental import pallas as pl
from jax.experimental.pallas import tpu as pltpu
from jax.sharding import Mesh
from jax.sharding import PartitionSpec as P

KVH = 8
GROUP = 8
HD = 128
BS = 128
GAIN_ROWS = 16

rope_theta = 500000.0

DP = ("x", "z", "ylo")
TP = ("yhi", "core")


def rope_tables(count):
    half_size = HD // 2
    positions = jnp.arange(count).astype(jnp.float32)
    inverse_freq = rope_theta ** (-(jnp.arange(half_size).astype(jnp.float32) * 2.0 / HD))
    angles = positions[:, None] * inverse_freq[None, :]
    cosine = jnp.cos(angles)
    sine_part = jnp.sin(angles)
    return (
        jnp.concatenate([cosine, cosine], axis=1),
        jnp.concatenate([-sine_part, sine_part], axis=1),
    )


def qkv_kernel(heads, slots, steps, rows_per_step, dest_ref, me_ref, normed_ref, w_ref, cos_ref,
               sin_ref, out_ref, acc_ref):
    step = pl.program_id(0)

    @pl.when(step == 0)
    def _():
        acc_ref[...] = jnp.zeros_like(acc_ref)

    for j in range(rows_per_step):
        row = step * rows_per_step + j
        y = jnp.dot(
            normed_ref[:, j * BS:(j + 1) * BS],
            w_ref[j * BS:(j + 1) * BS, :],
            preferred_element_type=jnp.float32,
        )
        for s in range(slots):
            d = dest_ref[row * slots + s]
            acc_ref[d] += y[:, s * BS:(s + 1) * BS]

    @pl.when(step == steps - 1)
    def _():
        cos = cos_ref[...]
        sin = sin_ref[...]
        for c in range(heads):
            x = acc_ref[c]
            if c < GROUP + 1:
                x = x * cos + pltpu.roll(x, HD // 2, 1) * sin
            out_ref[:, c * BS:(c + 1) * BS] = x.astype(out_ref.dtype)


def block_sparse_qkv(dest, me, normed, w, cos, sin, heads, slots):
    pieces, tokens, piece_features = normed.shape
    steps = pieces
    rows_per_step = piece_features // BS
    kernel = functools.partial(qkv_kernel, heads, slots, steps, rows_per_step)
    flops = 2 * tokens * pieces * piece_features * slots * BS
    bytes_accessed = normed.size * 2 + w.size * 2 + tokens * heads * BS * 2
    return pl.pallas_call(
        kernel,
        out_shape=jax.ShapeDtypeStruct((tokens, heads * BS), jnp.bfloat16),
        grid_spec=pltpu.PrefetchScalarGridSpec(
            num_scalar_prefetch=2,
            grid=(steps,),
            in_specs=[
                pl.BlockSpec((None, tokens, piece_features),
                             lambda i, d, m: ((m[0] - i + steps) % steps, 0, 0)),
                pl.BlockSpec((piece_features, slots * BS), lambda i, d, m: (i, 0)),
                pl.BlockSpec((tokens, HD), lambda i, d, m: (0, 0)),
                pl.BlockSpec((tokens, HD), lambda i, d, m: (0, 0)),
            ],
            out_specs=pl.BlockSpec((tokens, heads * BS), lambda i, d, m: (0, 0)),
            scratch_shapes=[pltpu.VMEM((heads + 1, tokens, BS), jnp.float32)],
        ),
        compiler_params=pltpu.CompilerParams(dimension_semantics=("arbitrary",)),
        cost_estimate=pl.CostEstimate(flops=flops, bytes_accessed=bytes_accessed, transcendentals=0),
    )(dest, me, normed, w, cos, sin)


def per_device(tokens, norm_gain, kept_blocks, block_cols, row_counts):
    tensor_count = lax.axis_size(TP)
    heads = KVH // tensor_count * (GROUP + 2) * HD // BS
    slots = block_cols.shape[1]
    token_count, piece_features = tokens.shape

    w = lax.all_gather(kept_blocks, "ylo", axis=0, tiled=True)
    w = lax.all_gather(w, ("x", "z"), axis=0, tiled=True)

    dest_here = jnp.where(jnp.arange(slots)[None, :] < row_counts, block_cols, heads)

    gain_rows = jnp.zeros((GAIN_ROWS, piece_features), tokens.dtype).at[0].set(norm_gain)
    piece = jnp.concatenate([tokens, gain_rows], axis=0)
    arrived = [piece]
    for k in range(1, tensor_count):
        shift = [(i, (i + k) % tensor_count) for i in range(tensor_count)]
        arrived.append(lax.ppermute(piece, TP, shift))
    stacked = jnp.stack(arrived)
    floats = stacked[:, :token_count].astype(jnp.float32)
    gains = stacked[:, token_count].astype(jnp.float32)
    mean_square = jnp.mean(floats * floats, axis=(0, 2))
    normed = (
        floats * lax.rsqrt(mean_square + 1e-05)[None, :, None] * gains[:, None, :]
    ).astype(jnp.bfloat16)
    dest_here, normed = lax.optimization_barrier((dest_here, normed))
    dest = lax.all_gather(dest_here, DP, axis=0, tiled=True).reshape(-1)
    me = lax.axis_index(TP).astype(jnp.int32).reshape(1)
    cos, sin = rope_tables(token_count)
    return block_sparse_qkv(dest, me, normed, w, cos, sin, heads, slots)


def solution(mesh):
    dp_size = mesh.shape["dp"]
    tp_size = mesh.shape["tensor"]
    fine = Mesh(mesh.devices.reshape(dp_size // 16, 8, 2, tp_size // 2, 2), DP + TP)
    spec = P(DP, TP)
    in_specs = (spec, P(TP), spec, spec, spec)
    return jax.shard_map(per_device, mesh=fine, in_specs=in_specs, out_specs=spec, check_vma=False)
```

```python
import functools

import jax
import jax.numpy as jnp
from jax import lax
from jax.experimental import pallas as pl
from jax.experimental.pallas import tpu as pltpu
from jax.sharding import Mesh
from jax.sharding import PartitionSpec as P

KVH = 8
GROUP = 8
HD = 128
BS = 128
GAIN_ROWS = 16
TABLE_ROWS = 8

rope_theta = 500000.0

DP = ("x", "z", "ylo")
TP = ("yhi", "core")


def rope_tables(count):
    half_size = HD // 2
    positions = jnp.arange(count).astype(jnp.float32)
    inverse_freq = rope_theta ** (-(jnp.arange(half_size).astype(jnp.float32) * 2.0 / HD))
    angles = positions[:, None] * inverse_freq[None, :]
    cosine = jnp.cos(angles)
    sine_part = jnp.sin(angles)
    return (
        jnp.concatenate([cosine, cosine], axis=1),
        jnp.concatenate([-sine_part, sine_part], axis=1),
    )


def qkv_kernel(heads, slots, steps, rows_per_step, dest_ref, me_ref, normed_ref, w_ref, cos_ref,
               sin_ref, out_ref, acc_ref):
    step = pl.program_id(0)

    @pl.when(step == 0)
    def _():
        acc_ref[...] = jnp.zeros_like(acc_ref)

    for j in range(rows_per_step):
        row = step * rows_per_step + j
        y = jnp.dot(
            normed_ref[:, j * BS:(j + 1) * BS],
            w_ref[j, :BS, :],
            preferred_element_type=jnp.float32,
        )
        for s in range(slots):
            d = dest_ref[row * slots + s]
            acc_ref[d] += y[:, s * BS:(s + 1) * BS]

    @pl.when(step == steps - 1)
    def _():
        cos = cos_ref[...]
        sin = sin_ref[...]
        for c in range(heads):
            x = acc_ref[c]
            if c < GROUP + 1:
                x = x * cos + pltpu.roll(x, HD // 2, 1) * sin
            out_ref[:, c * BS:(c + 1) * BS] = x.astype(out_ref.dtype)


def block_sparse_qkv(dest, me, normed, w, cos, sin, heads, slots):
    pieces, tokens, piece_features = normed.shape
    steps = pieces
    rows_per_step = piece_features // BS
    kernel = functools.partial(qkv_kernel, heads, slots, steps, rows_per_step)
    flops = 2 * tokens * pieces * piece_features * slots * BS
    bytes_accessed = normed.size * 2 + w.size * 2 + tokens * heads * BS * 2
    return pl.pallas_call(
        kernel,
        out_shape=jax.ShapeDtypeStruct((tokens, heads * BS), jnp.bfloat16),
        grid_spec=pltpu.PrefetchScalarGridSpec(
            num_scalar_prefetch=2,
            grid=(steps,),
            in_specs=[
                pl.BlockSpec((None, tokens, piece_features),
                             lambda i, d, m: ((m[0] - i + steps) % steps, 0, 0)),
                pl.BlockSpec((rows_per_step, w.shape[1], slots * BS), lambda i, d, m: (i, 0, 0)),
                pl.BlockSpec((tokens, HD), lambda i, d, m: (0, 0)),
                pl.BlockSpec((tokens, HD), lambda i, d, m: (0, 0)),
            ],
            out_specs=pl.BlockSpec((tokens, heads * BS), lambda i, d, m: (0, 0)),
            scratch_shapes=[pltpu.VMEM((heads + 1, tokens, BS), jnp.float32)],
        ),
        compiler_params=pltpu.CompilerParams(dimension_semantics=("arbitrary",)),
        cost_estimate=pl.CostEstimate(flops=flops, bytes_accessed=bytes_accessed, transcendentals=0),
    )(dest, me, normed, w, cos, sin)


def per_device(tokens, norm_gain, kept_blocks, block_cols, row_counts):
    tensor_count = lax.axis_size(TP)
    heads = KVH // tensor_count * (GROUP + 2) * HD // BS
    slots = block_cols.shape[1]
    token_count, piece_features = tokens.shape

    dest_here = jnp.where(jnp.arange(slots)[None, :] < row_counts, block_cols, heads)
    table_rows = jnp.zeros((TABLE_ROWS, kept_blocks.shape[1]), kept_blocks.dtype)
    table_rows = table_rows.at[0, :slots].set(dest_here[0].astype(kept_blocks.dtype))
    piece = jnp.concatenate([kept_blocks, table_rows], axis=0)
    w = lax.all_gather(piece, "ylo", axis=0, tiled=True)
    w = lax.all_gather(w, ("x", "z"), axis=0, tiled=True)
    w = w.reshape(-1, BS + TABLE_ROWS, kept_blocks.shape[1])
    dest = w[:, BS, :slots].astype(jnp.int32).reshape(-1)

    gain_rows = jnp.zeros((GAIN_ROWS, piece_features), tokens.dtype).at[0].set(norm_gain)
    piece = jnp.concatenate([tokens, gain_rows], axis=0)
    arrived = [piece]
    for k in range(1, tensor_count):
        shift = [(i, (i + k) % tensor_count) for i in range(tensor_count)]
        arrived.append(lax.ppermute(piece, TP, shift))
    stacked = jnp.stack(arrived)
    floats = stacked[:, :token_count].astype(jnp.float32)
    gains = stacked[:, token_count].astype(jnp.float32)
    mean_square = jnp.mean(floats * floats, axis=(0, 2))
    normed = (
        floats * lax.rsqrt(mean_square + 1e-05)[None, :, None] * gains[:, None, :]
    ).astype(jnp.bfloat16)
    me = lax.axis_index(TP).astype(jnp.int32).reshape(1)
    cos, sin = rope_tables(token_count)
    return block_sparse_qkv(dest, me, normed, w, cos, sin, heads, slots)


def solution(mesh):
    dp_size = mesh.shape["dp"]
    tp_size = mesh.shape["tensor"]
    fine = Mesh(mesh.devices.reshape(dp_size // 16, 8, 2, tp_size // 2, 2), DP + TP)
    spec = P(DP, TP)
    in_specs = (spec, P(TP), spec, spec, spec)
    return jax.shard_map(per_device, mesh=fine, in_specs=in_specs, out_specs=spec, check_vma=False)
```

```python
import functools

import jax
import jax.numpy as jnp
from jax import lax
from jax.experimental import pallas as pl
from jax.experimental.pallas import tpu as pltpu
from jax.sharding import Mesh
from jax.sharding import PartitionSpec as P

KVH = 8
GROUP = 8
HD = 128
BS = 128
TABLE_ROWS = 8

rope_theta = 500000.0

DP = ("x", "z", "ylo")
TP = ("yhi", "core")


def rotate(mixed, positions):
    row_count = mixed.shape[0]
    head_view = mixed.reshape(row_count, -1, GROUP + 2, HD)
    half_size = HD // 2
    inverse_freq = rope_theta ** (-(jnp.arange(half_size).astype(jnp.float32) * 2.0 / HD))
    angles = positions[:, None] * inverse_freq[None, :]
    cosine = jnp.cos(angles)[:, None, None, :]
    sine_part = jnp.sin(angles)[:, None, None, :]
    first_half = head_view[..., :half_size]
    second = head_view[..., half_size:]
    turned = jnp.concatenate(
        [first_half * cosine - second * sine_part, second * cosine + first_half * sine_part],
        axis=-1,
    )
    rotated_heads = (jnp.arange(GROUP + 2) < GROUP + 1)[None, None, :, None]
    return jnp.where(rotated_heads, turned, head_view).reshape(row_count, -1)


def partial_kernel(heads, slots, steps, rows_per_step, dest_ref, order_ref, x_ref, w_ref, out_ref,
                   acc_ref):
    step = pl.program_id(0)

    @pl.when(step == 0)
    def _():
        acc_ref[...] = jnp.zeros_like(acc_ref)

    for j in range(rows_per_step):
        row = step * rows_per_step + j
        features = x_ref[:, j * BS:(j + 1) * BS]
        for s in range(slots):
            d = dest_ref[row * slots + s]
            acc_ref[d] += jnp.dot(
                features, w_ref[j, :BS, s * BS:(s + 1) * BS], preferred_element_type=jnp.float32
            )

    @pl.when(step == steps - 1)
    def _():
        for c in range(heads):
            out_ref[:, c * BS:(c + 1) * BS] = acc_ref[c]


def block_sparse_partial(dest, order, pieces, w, token_half, heads, slots):
    count, both, piece_features = pieces.shape
    tokens = both // 2
    rows_per_step = piece_features // BS
    kernel = functools.partial(partial_kernel, heads, slots, count, rows_per_step)
    flops = 2 * tokens * count * piece_features * slots * BS
    bytes_accessed = tokens * count * piece_features * 2 + w.size * 2 + tokens * heads * BS * 4
    return pl.pallas_call(
        kernel,
        out_shape=jax.ShapeDtypeStruct((tokens, heads * BS), jnp.float32),
        grid_spec=pltpu.PrefetchScalarGridSpec(
            num_scalar_prefetch=2,
            grid=(count,),
            in_specs=[
                pl.BlockSpec((None, tokens, piece_features),
                             lambda i, d, o: (o[i], token_half, 0)),
                pl.BlockSpec((rows_per_step, w.shape[1], slots * BS), lambda i, d, o: (i, 0, 0)),
            ],
            out_specs=pl.BlockSpec((tokens, heads * BS), lambda i, d, o: (0, 0)),
            scratch_shapes=[pltpu.VMEM((heads + 1, tokens, BS), jnp.float32)],
        ),
        compiler_params=pltpu.CompilerParams(dimension_semantics=("arbitrary",)),
        cost_estimate=pl.CostEstimate(flops=flops, bytes_accessed=bytes_accessed, transcendentals=0),
    )(dest, order, pieces, w)


def ring(size, step):
    return [(i, (i + step) % size) for i in range(size)]


def per_device(tokens, norm_gain, kept_blocks, block_cols, row_counts):
    tensor_count = lax.axis_size(TP)
    heads = KVH // tensor_count * (GROUP + 2) * HD // BS
    slots = block_cols.shape[1]
    pair = lax.axis_size("ylo")
    chips = lax.axis_size("yhi")
    cores = lax.axis_size("core")
    half = lax.axis_index("ylo")
    token_count, piece_features = tokens.shape
    width = kept_blocks.shape[1]

    dest_here = jnp.where(jnp.arange(slots)[None, :] < row_counts, block_cols, heads)
    table_rows = jnp.zeros((TABLE_ROWS, width), kept_blocks.dtype)
    table_rows = table_rows.at[0, :slots].set(dest_here[0].astype(kept_blocks.dtype))
    w = lax.all_gather(jnp.concatenate([kept_blocks, table_rows], axis=0), ("x", "z"), axis=0, tiled=True)
    w = w.reshape(-1, BS + TABLE_ROWS, width)
    dest = w[:, BS, :slots].astype(jnp.int32).reshape(-1)

    floats = tokens.astype(jnp.float32)
    square_sum = lax.psum(jnp.sum(floats * floats, axis=-1), TP)
    scale = lax.rsqrt(square_sum / (piece_features * tensor_count) + 1e-05)
    normed = (floats * scale[:, None] * norm_gain.astype(jnp.float32)).astype(jnp.bfloat16)
    by_parity = normed.reshape(token_count, -1, pair, BS)
    even = by_parity[:, :, 0, :].reshape(token_count, -1)
    odd = by_parity[:, :, 1, :].reshape(token_count, -1)
    mine = jnp.where(half == 0, even, odd)
    theirs = jnp.where(half == 0, odd, even)
    partner_rows = lax.ppermute(theirs, "ylo", ring(pair, 1))
    piece = jnp.concatenate([mine, partner_rows], axis=0)

    from_below = lax.ppermute(piece, "yhi", ring(chips, 1))
    from_above = lax.ppermute(piece, "yhi", ring(chips, -1))
    cut = piece.shape[1] // 2
    far_low = lax.ppermute(from_below[:, :cut], "yhi", ring(chips, 1))
    far_high = lax.ppermute(from_above[:, cut:], "yhi", ring(chips, -1))
    far = jnp.concatenate([far_low, far_high], axis=1)
    own_core = jnp.stack([piece, from_below, from_above, far])
    other_core = lax.ppermute(own_core, "core", ring(cores, 1))
    pieces = jnp.concatenate([own_core, other_core], axis=0)

    chip = lax.axis_index("yhi")
    core = lax.axis_index("core")
    offsets = jnp.array([0, -1, 1, 2], jnp.int32)
    entry_chip = jnp.concatenate([(chip + offsets) % chips] * 2)
    entry_core = jnp.concatenate([jnp.full((4,), core), jnp.full((4,), (core + 1) % cores)])
    holder = entry_chip * cores + entry_core
    order = jnp.zeros((tensor_count,), jnp.int32).at[holder].set(jnp.arange(tensor_count, dtype=jnp.int32))

    partner_partial = block_sparse_partial(dest, order, pieces, w, 1, heads, slots)
    returned = lax.ppermute(partner_partial, "ylo", ring(pair, 1))
    own_partial = block_sparse_partial(dest, order, pieces, w, 0, heads, slots)
    mixed = own_partial + returned
    positions = jnp.arange(token_count).astype(jnp.float32)
    return rotate(mixed, positions).astype(jnp.bfloat16)


def solution(mesh):
    dp_size = mesh.shape["dp"]
    tp_size = mesh.shape["tensor"]
    fine = Mesh(mesh.devices.reshape(dp_size // 16, 8, 2, tp_size // 2, 2), DP + TP)
    spec = P(DP, TP)
    in_specs = (spec, P(TP), spec, spec, spec)
    return jax.shard_map(per_device, mesh=fine, in_specs=in_specs, out_specs=spec, check_vma=False)
```

```python
import functools

import jax
import jax.numpy as jnp
from jax import lax
from jax.experimental import pallas as pl
from jax.experimental.pallas import tpu as pltpu
from jax.sharding import Mesh
from jax.sharding import PartitionSpec as P

KVH = 8
GROUP = 8
HD = 128
BS = 128
TABLE_ROWS = 8

rope_theta = 500000.0

DP = ("x", "z", "ylo")
TP = ("yhi", "core")


def rotate(mixed, positions):
    row_count = mixed.shape[0]
    head_view = mixed.reshape(row_count, -1, GROUP + 2, HD)
    half_size = HD // 2
    inverse_freq = rope_theta ** (-(jnp.arange(half_size).astype(jnp.float32) * 2.0 / HD))
    angles = positions[:, None] * inverse_freq[None, :]
    cosine = jnp.cos(angles)[:, None, None, :]
    sine_part = jnp.sin(angles)[:, None, None, :]
    first_half = head_view[..., :half_size]
    second = head_view[..., half_size:]
    turned = jnp.concatenate(
        [first_half * cosine - second * sine_part, second * cosine + first_half * sine_part],
        axis=-1,
    )
    rotated_heads = (jnp.arange(GROUP + 2) < GROUP + 1)[None, None, :, None]
    return jnp.where(rotated_heads, turned, head_view).reshape(row_count, -1)


def partial_kernel(heads, slots, steps, rows_per_step, dest_ref, order_ref, x_ref, w_ref, out_ref,
                   acc_ref):
    step = pl.program_id(0)

    @pl.when(step == 0)
    def _():
        acc_ref[...] = jnp.zeros_like(acc_ref)

    for j in range(rows_per_step):
        row = step * rows_per_step + j
        features = x_ref[:, j * BS:(j + 1) * BS]
        for s in range(slots):
            d = dest_ref[row * slots + s]
            acc_ref[d] += jnp.dot(
                features, w_ref[j, :BS, s * BS:(s + 1) * BS], preferred_element_type=jnp.float32
            )

    @pl.when(step == steps - 1)
    def _():
        for c in range(heads):
            out_ref[:, c * BS:(c + 1) * BS] = acc_ref[c].astype(out_ref.dtype)


def block_sparse_partial(dest, order, pieces, w, token_half, heads, slots, out_dtype):
    count, both, piece_features = pieces.shape
    tokens = both // 2
    rows_per_step = piece_features // BS
    kernel = functools.partial(partial_kernel, heads, slots, count, rows_per_step)
    flops = 2 * tokens * count * piece_features * slots * BS
    bytes_accessed = (tokens * count * piece_features * 2 + w.size * 2
                      + tokens * heads * BS * jnp.dtype(out_dtype).itemsize)
    return pl.pallas_call(
        kernel,
        out_shape=jax.ShapeDtypeStruct((tokens, heads * BS), out_dtype),
        grid_spec=pltpu.PrefetchScalarGridSpec(
            num_scalar_prefetch=2,
            grid=(count,),
            in_specs=[
                pl.BlockSpec((None, tokens, piece_features),
                             lambda i, d, o: (o[i], token_half, 0)),
                pl.BlockSpec((rows_per_step, w.shape[1], slots * BS), lambda i, d, o: (i, 0, 0)),
            ],
            out_specs=pl.BlockSpec((tokens, heads * BS), lambda i, d, o: (0, 0)),
            scratch_shapes=[pltpu.VMEM((heads + 1, tokens, BS), jnp.float32)],
        ),
        compiler_params=pltpu.CompilerParams(dimension_semantics=("arbitrary",)),
        cost_estimate=pl.CostEstimate(flops=flops, bytes_accessed=bytes_accessed, transcendentals=0),
    )(dest, order, pieces, w)


def ring(size, step):
    return [(i, (i + step) % size) for i in range(size)]


def per_device(tokens, norm_gain, kept_blocks, block_cols, row_counts):
    tensor_count = lax.axis_size(TP)
    heads = KVH // tensor_count * (GROUP + 2) * HD // BS
    slots = block_cols.shape[1]
    pair = lax.axis_size("ylo")
    chips = lax.axis_size("yhi")
    cores = lax.axis_size("core")
    half = lax.axis_index("ylo")
    token_count, piece_features = tokens.shape
    width = kept_blocks.shape[1]

    dest_here = jnp.where(jnp.arange(slots)[None, :] < row_counts, block_cols, heads)
    table_rows = jnp.zeros((TABLE_ROWS, width), kept_blocks.dtype)
    table_rows = table_rows.at[0, :slots].set(dest_here[0].astype(kept_blocks.dtype))
    w = lax.all_gather(jnp.concatenate([kept_blocks, table_rows], axis=0), ("x", "z"), axis=0, tiled=True)
    w = w.reshape(-1, BS + TABLE_ROWS, width)
    dest = w[:, BS, :slots].astype(jnp.int32).reshape(-1)

    floats = tokens.astype(jnp.float32)
    square_sum = lax.psum(jnp.sum(floats * floats, axis=-1), TP)
    scale = lax.rsqrt(square_sum / (piece_features * tensor_count) + 1e-05)
    normed = (floats * scale[:, None] * norm_gain.astype(jnp.float32)).astype(jnp.bfloat16)
    by_parity = normed.reshape(token_count, -1, pair, BS)
    even = by_parity[:, :, 0, :].reshape(token_count, -1)
    odd = by_parity[:, :, 1, :].reshape(token_count, -1)
    mine = jnp.where(half == 0, even, odd)
    theirs = jnp.where(half == 0, odd, even)
    partner_rows = lax.ppermute(theirs, "ylo", ring(pair, 1))
    piece = jnp.concatenate([mine, partner_rows], axis=0)

    from_below = lax.ppermute(piece, "yhi", ring(chips, 1))
    from_above = lax.ppermute(piece, "yhi", ring(chips, -1))
    cut = piece.shape[1] // 2
    far_low = lax.ppermute(from_below[:, :cut], "yhi", ring(chips, 1))
    far_high = lax.ppermute(from_above[:, cut:], "yhi", ring(chips, -1))
    far = jnp.concatenate([far_low, far_high], axis=1)
    own_core = jnp.stack([piece, from_below, from_above, far])
    other_core = lax.ppermute(own_core, "core", ring(cores, 1))
    pieces = jnp.concatenate([own_core, other_core], axis=0)

    chip = lax.axis_index("yhi")
    core = lax.axis_index("core")
    offsets = jnp.array([0, -1, 1, 2], jnp.int32)
    entry_chip = jnp.concatenate([(chip + offsets) % chips] * 2)
    entry_core = jnp.concatenate([jnp.full((4,), core), jnp.full((4,), (core + 1) % cores)])
    holder = entry_chip * cores + entry_core
    order = jnp.zeros((tensor_count,), jnp.int32).at[holder].set(jnp.arange(tensor_count, dtype=jnp.int32))

    partner_partial = block_sparse_partial(dest, order, pieces, w, 1, heads, slots, jnp.bfloat16)
    returned = lax.ppermute(partner_partial, "ylo", ring(pair, 1))
    own_partial = block_sparse_partial(dest, order, pieces, w, 0, heads, slots, jnp.float32)
    mixed = own_partial + returned.astype(jnp.float32)
    positions = jnp.arange(token_count).astype(jnp.float32)
    return rotate(mixed, positions).astype(jnp.bfloat16)


def solution(mesh):
    dp_size = mesh.shape["dp"]
    tp_size = mesh.shape["tensor"]
    fine = Mesh(mesh.devices.reshape(dp_size // 16, 8, 2, tp_size // 2, 2), DP + TP)
    spec = P(DP, TP)
    in_specs = (spec, P(TP), spec, spec, spec)
    return jax.shard_map(per_device, mesh=fine, in_specs=in_specs, out_specs=spec, check_vma=False)
```

```python
import functools

import jax
import jax.numpy as jnp
from jax import lax
from jax.experimental import pallas as pl
from jax.experimental.pallas import tpu as pltpu
from jax.sharding import Mesh
from jax.sharding import PartitionSpec as P

KVH = 8
GROUP = 8
HD = 128
BS = 128
TABLE_ROWS = 8

rope_theta = 500000.0

DP = ("x", "z", "ylo")
TP = ("yhi", "core")


def rotate(mixed, positions):
    row_count = mixed.shape[0]
    head_view = mixed.reshape(row_count, -1, GROUP + 2, HD)
    half_size = HD // 2
    inverse_freq = rope_theta ** (-(jnp.arange(half_size).astype(jnp.float32) * 2.0 / HD))
    angles = positions[:, None] * inverse_freq[None, :]
    cosine = jnp.cos(angles)[:, None, None, :]
    sine_part = jnp.sin(angles)[:, None, None, :]
    first_half = head_view[..., :half_size]
    second = head_view[..., half_size:]
    turned = jnp.concatenate(
        [first_half * cosine - second * sine_part, second * cosine + first_half * sine_part],
        axis=-1,
    )
    rotated_heads = (jnp.arange(GROUP + 2) < GROUP + 1)[None, None, :, None]
    return jnp.where(rotated_heads, turned, head_view).reshape(row_count, -1)


def partial_kernel(heads, slots, steps, rows_per_piece, per_step, dest_ref, order_ref, *refs):
    x_refs = refs[:per_step]
    w_ref, out_ref, acc_ref = refs[per_step:]
    step = pl.program_id(0)

    @pl.when(step == 0)
    def _():
        acc_ref[...] = jnp.zeros_like(acc_ref)

    for p in range(per_step):
        for j in range(rows_per_piece):
            local = p * rows_per_piece + j
            row = step * per_step * rows_per_piece + local
            features = x_refs[p][:, j * BS:(j + 1) * BS]
            for s in range(slots):
                d = dest_ref[row * slots + s]
                acc_ref[d] += jnp.dot(
                    features, w_ref[local, :BS, s * BS:(s + 1) * BS],
                    preferred_element_type=jnp.float32,
                )

    @pl.when(step == steps - 1)
    def _():
        for c in range(heads):
            out_ref[:, c * BS:(c + 1) * BS] = acc_ref[c].astype(out_ref.dtype)


def block_sparse_partial(dest, order, pieces, w, token_half, heads, slots, out_dtype):
    count, both, piece_features = pieces.shape
    tokens = both // 2
    rows_per_piece = piece_features // BS
    per_step = 2 if count % 2 == 0 else 1
    steps = count // per_step
    kernel = functools.partial(partial_kernel, heads, slots, steps, rows_per_piece, per_step)
    flops = 2 * tokens * count * piece_features * slots * BS
    bytes_accessed = (tokens * count * piece_features * 2 + w.size * 2
                      + tokens * heads * BS * jnp.dtype(out_dtype).itemsize)

    def piece_map(p):
        return lambda i, d, o: (o[i * per_step + p], token_half, 0)

    return pl.pallas_call(
        kernel,
        out_shape=jax.ShapeDtypeStruct((tokens, heads * BS), out_dtype),
        grid_spec=pltpu.PrefetchScalarGridSpec(
            num_scalar_prefetch=2,
            grid=(steps,),
            in_specs=[pl.BlockSpec((None, tokens, piece_features), piece_map(p)) for p in range(per_step)]
            + [pl.BlockSpec((per_step * rows_per_piece, w.shape[1], slots * BS), lambda i, d, o: (i, 0, 0))],
            out_specs=pl.BlockSpec((tokens, heads * BS), lambda i, d, o: (0, 0)),
            scratch_shapes=[pltpu.VMEM((heads + 1, tokens, BS), jnp.float32)],
        ),
        compiler_params=pltpu.CompilerParams(dimension_semantics=("arbitrary",)),
        cost_estimate=pl.CostEstimate(flops=flops, bytes_accessed=bytes_accessed, transcendentals=0),
    )(dest, order, *([pieces] * per_step), w)


def ring(size, step):
    return [(i, (i + step) % size) for i in range(size)]


def per_device(tokens, norm_gain, kept_blocks, block_cols, row_counts):
    tensor_count = lax.axis_size(TP)
    heads = KVH // tensor_count * (GROUP + 2) * HD // BS
    slots = block_cols.shape[1]
    pair = lax.axis_size("ylo")
    chips = lax.axis_size("yhi")
    cores = lax.axis_size("core")
    half = lax.axis_index("ylo")
    token_count, piece_features = tokens.shape
    width = kept_blocks.shape[1]

    dest_here = jnp.where(jnp.arange(slots)[None, :] < row_counts, block_cols, heads)
    table_rows = jnp.zeros((TABLE_ROWS, width), kept_blocks.dtype)
    table_rows = table_rows.at[0, :slots].set(dest_here[0].astype(kept_blocks.dtype))
    w = lax.all_gather(jnp.concatenate([kept_blocks, table_rows], axis=0), ("x", "z"), axis=0, tiled=True)
    w = w.reshape(-1, BS + TABLE_ROWS, width)
    dest = w[:, BS, :slots].astype(jnp.int32).reshape(-1)

    floats = tokens.astype(jnp.float32)
    square_sum = lax.psum(jnp.sum(floats * floats, axis=-1), TP)
    scale = lax.rsqrt(square_sum / (piece_features * tensor_count) + 1e-05)
    normed = (floats * scale[:, None] * norm_gain.astype(jnp.float32)).astype(jnp.bfloat16)
    by_parity = normed.reshape(token_count, -1, pair, BS)
    even = by_parity[:, :, 0, :].reshape(token_count, -1)
    odd = by_parity[:, :, 1, :].reshape(token_count, -1)
    mine = jnp.where(half == 0, even, odd)
    theirs = jnp.where(half == 0, odd, even)
    partner_rows = lax.ppermute(theirs, "ylo", ring(pair, 1))
    piece = jnp.concatenate([mine, partner_rows], axis=0)

    from_below = lax.ppermute(piece, "yhi", ring(chips, 1))
    from_above = lax.ppermute(piece, "yhi", ring(chips, -1))
    cut = piece.shape[1] // 2
    far_low = lax.ppermute(from_below[:, :cut], "yhi", ring(chips, 1))
    far_high = lax.ppermute(from_above[:, cut:], "yhi", ring(chips, -1))
    far = jnp.concatenate([far_low, far_high], axis=1)
    own_core = jnp.stack([piece, from_below, from_above, far])
    other_core = lax.ppermute(own_core, "core", ring(cores, 1))
    pieces = jnp.concatenate([own_core, other_core], axis=0)

    chip = lax.axis_index("yhi")
    core = lax.axis_index("core")
    offsets = jnp.array([0, -1, 1, 2], jnp.int32)
    entry_chip = jnp.concatenate([(chip + offsets) % chips] * 2)
    entry_core = jnp.concatenate([jnp.full((4,), core), jnp.full((4,), (core + 1) % cores)])
    holder = entry_chip * cores + entry_core
    order = jnp.zeros((tensor_count,), jnp.int32).at[holder].set(jnp.arange(tensor_count, dtype=jnp.int32))

    partner_partial = block_sparse_partial(dest, order, pieces, w, 1, heads, slots, jnp.bfloat16)
    returned = lax.ppermute(partner_partial, "ylo", ring(pair, 1))
    own_partial = block_sparse_partial(dest, order, pieces, w, 0, heads, slots, jnp.float32)
    mixed = own_partial + returned.astype(jnp.float32)
    positions = jnp.arange(token_count).astype(jnp.float32)
    return rotate(mixed, positions).astype(jnp.bfloat16)


def solution(mesh):
    dp_size = mesh.shape["dp"]
    tp_size = mesh.shape["tensor"]
    fine = Mesh(mesh.devices.reshape(dp_size // 16, 8, 2, tp_size // 2, 2), DP + TP)
    spec = P(DP, TP)
    in_specs = (spec, P(TP), spec, spec, spec)
    return jax.shard_map(per_device, mesh=fine, in_specs=in_specs, out_specs=spec, check_vma=False)
```

```python
import functools

import jax
import jax.numpy as jnp
from jax import lax
from jax.experimental import pallas as pl
from jax.experimental.pallas import tpu as pltpu
from jax.sharding import Mesh
from jax.sharding import PartitionSpec as P

KVH = 8
GROUP = 8
HD = 128
BS = 128
TABLE_ROWS = 8

rope_theta = 500000.0

DP = ("x", "z", "ylo")
TP = ("yhi", "core")


def rotate(mixed, positions):
    row_count = mixed.shape[0]
    head_view = mixed.reshape(row_count, -1, GROUP + 2, HD)
    half_size = HD // 2
    inverse_freq = rope_theta ** (-(jnp.arange(half_size).astype(jnp.float32) * 2.0 / HD))
    angles = positions[:, None] * inverse_freq[None, :]
    cosine = jnp.cos(angles)[:, None, None, :]
    sine_part = jnp.sin(angles)[:, None, None, :]
    first_half = head_view[..., :half_size]
    second = head_view[..., half_size:]
    turned = jnp.concatenate(
        [first_half * cosine - second * sine_part, second * cosine + first_half * sine_part],
        axis=-1,
    )
    rotated_heads = (jnp.arange(GROUP + 2) < GROUP + 1)[None, None, :, None]
    return jnp.where(rotated_heads, turned, head_view).reshape(row_count, -1)


def partial_kernel(heads, slots, steps, rows_per_piece, per_step, dest_ref, order_ref, *refs):
    x_refs = refs[:per_step]
    w_ref, out_ref, acc_ref = refs[per_step:]
    step = pl.program_id(0)

    @pl.when(step == 0)
    def _():
        acc_ref[...] = jnp.zeros_like(acc_ref)

    for p in range(per_step):
        for j in range(rows_per_piece):
            local = p * rows_per_piece + j
            row = step * per_step * rows_per_piece + local
            features = x_refs[p][:, j * BS:(j + 1) * BS]
            for s in range(slots):
                d = dest_ref[row, s]
                acc_ref[d] += jnp.dot(
                    features, w_ref[local, :BS, s * BS:(s + 1) * BS],
                    preferred_element_type=jnp.float32,
                )

    @pl.when(step == steps - 1)
    def _():
        for c in range(heads):
            out_ref[:, c * BS:(c + 1) * BS] = acc_ref[c].astype(out_ref.dtype)


def block_sparse_partial(dest, order, pieces, w, token_half, heads, slots, out_dtype):
    count, both, piece_features = pieces.shape
    tokens = both // 2
    rows_per_piece = piece_features // BS
    per_step = 2 if count % 2 == 0 else 1
    steps = count // per_step
    kernel = functools.partial(partial_kernel, heads, slots, steps, rows_per_piece, per_step)
    flops = 2 * tokens * count * piece_features * slots * BS
    bytes_accessed = (tokens * count * piece_features * 2 + w.size * 2
                      + tokens * heads * BS * jnp.dtype(out_dtype).itemsize)

    def piece_map(p):
        return lambda i, d, o: (o[i * per_step + p], token_half, 0)

    return pl.pallas_call(
        kernel,
        out_shape=jax.ShapeDtypeStruct((tokens, heads * BS), out_dtype),
        grid_spec=pltpu.PrefetchScalarGridSpec(
            num_scalar_prefetch=2,
            grid=(steps,),
            in_specs=[pl.BlockSpec((None, tokens, piece_features), piece_map(p)) for p in range(per_step)]
            + [pl.BlockSpec((per_step * rows_per_piece, w.shape[1], slots * BS), lambda i, d, o: (i, 0, 0))],
            out_specs=pl.BlockSpec((tokens, heads * BS), lambda i, d, o: (0, 0)),
            scratch_shapes=[pltpu.VMEM((heads + 1, tokens, BS), jnp.float32)],
        ),
        compiler_params=pltpu.CompilerParams(dimension_semantics=("arbitrary",)),
        cost_estimate=pl.CostEstimate(flops=flops, bytes_accessed=bytes_accessed, transcendentals=0),
    )(dest, order, *([pieces] * per_step), w)


def rope_tables(count):
    half_size = HD // 2
    positions = jnp.arange(count).astype(jnp.float32)
    inverse_freq = rope_theta ** (-(jnp.arange(half_size).astype(jnp.float32) * 2.0 / HD))
    angles = positions[:, None] * inverse_freq[None, :]
    cosine = jnp.cos(angles)
    sine_part = jnp.sin(angles)
    return (
        jnp.concatenate([cosine, cosine], axis=1),
        jnp.concatenate([-sine_part, sine_part], axis=1),
    )


def finish_kernel(heads, own_ref, returned_ref, cos_ref, sin_ref, out_ref):
    cos = cos_ref[...]
    sin = sin_ref[...]
    for c in range(heads):
        block = slice(c * BS, (c + 1) * BS)
        x = own_ref[:, block] + returned_ref[:, block].astype(jnp.float32)
        if c < GROUP + 1:
            x = x * cos + pltpu.roll(x, HD // 2, 1) * sin
        out_ref[:, block] = x.astype(out_ref.dtype)


def finish(own, returned, heads):
    tokens = own.shape[0]
    cos, sin = rope_tables(tokens)
    return pl.pallas_call(
        functools.partial(finish_kernel, heads),
        out_shape=jax.ShapeDtypeStruct(own.shape, jnp.bfloat16),
    )(own, returned, cos, sin)


def ring(size, step):
    return [(i, (i + step) % size) for i in range(size)]


def per_device(tokens, norm_gain, kept_blocks, block_cols, row_counts):
    tensor_count = lax.axis_size(TP)
    heads = KVH // tensor_count * (GROUP + 2) * HD // BS
    slots = block_cols.shape[1]
    pair = lax.axis_size("ylo")
    chips = lax.axis_size("yhi")
    cores = lax.axis_size("core")
    half = lax.axis_index("ylo")
    token_count, piece_features = tokens.shape
    width = kept_blocks.shape[1]

    dest_here = jnp.where(jnp.arange(slots)[None, :] < row_counts, block_cols, heads)
    table_rows = jnp.zeros((TABLE_ROWS, width), kept_blocks.dtype)
    table_rows = table_rows.at[0, :slots].set(dest_here[0].astype(kept_blocks.dtype))
    w = lax.all_gather(jnp.concatenate([kept_blocks, table_rows], axis=0), ("x", "z"), axis=0, tiled=True)
    w = w.reshape(-1, BS + TABLE_ROWS, width)
    dest = w[:, BS, :slots].astype(jnp.int32)

    floats = tokens.astype(jnp.float32)
    square_sum = lax.psum(jnp.sum(floats * floats, axis=-1), TP)
    scale = lax.rsqrt(square_sum / (piece_features * tensor_count) + 1e-05)
    normed = (floats * scale[:, None] * norm_gain.astype(jnp.float32)).astype(jnp.bfloat16)
    by_parity = normed.reshape(token_count, -1, pair, BS)
    even = by_parity[:, :, 0, :].reshape(token_count, -1)
    odd = by_parity[:, :, 1, :].reshape(token_count, -1)
    mine = jnp.where(half == 0, even, odd)
    theirs = jnp.where(half == 0, odd, even)
    partner_rows = lax.ppermute(theirs, "ylo", ring(pair, 1))
    piece = jnp.concatenate([mine, partner_rows], axis=0)

    from_below = lax.ppermute(piece, "yhi", ring(chips, 1))
    from_above = lax.ppermute(piece, "yhi", ring(chips, -1))
    cut = piece.shape[1] // 2
    far_low = lax.ppermute(from_below[:, :cut], "yhi", ring(chips, 1))
    far_high = lax.ppermute(from_above[:, cut:], "yhi", ring(chips, -1))
    far = jnp.concatenate([far_low, far_high], axis=1)
    own_core = jnp.stack([piece, from_below, from_above, far])
    other_core = lax.ppermute(own_core, "core", ring(cores, 1))
    pieces = jnp.concatenate([own_core, other_core], axis=0)

    chip = lax.axis_index("yhi")
    core = lax.axis_index("core")
    offsets = jnp.array([0, -1, 1, 2], jnp.int32)
    entry_chip = jnp.concatenate([(chip + offsets) % chips] * 2)
    entry_core = jnp.concatenate([jnp.full((4,), core), jnp.full((4,), (core + 1) % cores)])
    holder = entry_chip * cores + entry_core
    order = jnp.zeros((tensor_count,), jnp.int32).at[holder].set(jnp.arange(tensor_count, dtype=jnp.int32))

    partner_partial = block_sparse_partial(dest, order, pieces, w, 1, heads, slots, jnp.bfloat16)
    returned = lax.ppermute(partner_partial, "ylo", ring(pair, 1))
    own_partial = block_sparse_partial(dest, order, pieces, w, 0, heads, slots, jnp.float32)
    return finish(own_partial, returned, heads)


def solution(mesh):
    dp_size = mesh.shape["dp"]
    tp_size = mesh.shape["tensor"]
    fine = Mesh(mesh.devices.reshape(dp_size // 16, 8, 2, tp_size // 2, 2), DP + TP)
    spec = P(DP, TP)
    in_specs = (spec, P(TP), spec, spec, spec)
    return jax.shard_map(per_device, mesh=fine, in_specs=in_specs, out_specs=spec, check_vma=False)
```

```python
import functools

import jax
import jax.numpy as jnp
from jax import lax
from jax.experimental import pallas as pl
from jax.experimental.pallas import tpu as pltpu
from jax.sharding import Mesh
from jax.sharding import PartitionSpec as P

KVH = 8
GROUP = 8
HD = 128
BS = 128
TABLE_ROWS = 8

rope_theta = 500000.0

DP = ("x", "z", "ylo")
TP = ("yhi", "core")


def rotate(mixed, positions):
    row_count = mixed.shape[0]
    head_view = mixed.reshape(row_count, -1, GROUP + 2, HD)
    half_size = HD // 2
    inverse_freq = rope_theta ** (-(jnp.arange(half_size).astype(jnp.float32) * 2.0 / HD))
    angles = positions[:, None] * inverse_freq[None, :]
    cosine = jnp.cos(angles)[:, None, None, :]
    sine_part = jnp.sin(angles)[:, None, None, :]
    first_half = head_view[..., :half_size]
    second = head_view[..., half_size:]
    turned = jnp.concatenate(
        [first_half * cosine - second * sine_part, second * cosine + first_half * sine_part],
        axis=-1,
    )
    rotated_heads = (jnp.arange(GROUP + 2) < GROUP + 1)[None, None, :, None]
    return jnp.where(rotated_heads, turned, head_view).reshape(row_count, -1)


def partial_kernel(heads, slots, steps, rows_per_piece, per_step, dest_ref, order_ref, *refs):
    x_refs = refs[:per_step]
    w_ref, out_ref, acc_ref = refs[per_step:]
    step = pl.program_id(0)

    @pl.when(step == 0)
    def _():
        acc_ref[...] = jnp.zeros_like(acc_ref)

    for p in range(per_step):
        for j in range(rows_per_piece):
            local = p * rows_per_piece + j
            row = step * per_step * rows_per_piece + local
            features = x_refs[p][:, j * BS:(j + 1) * BS]
            for s in range(slots):
                d = dest_ref[row * slots + s]
                acc_ref[d] += jnp.dot(
                    features, w_ref[local, :BS, s * BS:(s + 1) * BS],
                    preferred_element_type=jnp.float32,
                )

    @pl.when(step == steps - 1)
    def _():
        for c in range(heads):
            out_ref[:, c * BS:(c + 1) * BS] = acc_ref[c].astype(out_ref.dtype)


def block_sparse_partial(dest, order, pieces, w, token_half, heads, slots, out_dtype):
    count, both, piece_features = pieces.shape
    tokens = both // 2
    rows_per_piece = piece_features // BS
    per_step = 4 if count % 4 == 0 else 1
    steps = count // per_step
    kernel = functools.partial(partial_kernel, heads, slots, steps, rows_per_piece, per_step)
    flops = 2 * tokens * count * piece_features * slots * BS
    bytes_accessed = (tokens * count * piece_features * 2 + w.size * 2
                      + tokens * heads * BS * jnp.dtype(out_dtype).itemsize)

    def piece_map(p):
        return lambda i, d, o: (o[i * per_step + p], token_half, 0)

    return pl.pallas_call(
        kernel,
        out_shape=jax.ShapeDtypeStruct((tokens, heads * BS), out_dtype),
        grid_spec=pltpu.PrefetchScalarGridSpec(
            num_scalar_prefetch=2,
            grid=(steps,),
            in_specs=[pl.BlockSpec((None, tokens, piece_features), piece_map(p)) for p in range(per_step)]
            + [pl.BlockSpec((per_step * rows_per_piece, w.shape[1], slots * BS), lambda i, d, o: (i, 0, 0))],
            out_specs=pl.BlockSpec((tokens, heads * BS), lambda i, d, o: (0, 0)),
            scratch_shapes=[pltpu.VMEM((heads + 1, tokens, BS), jnp.float32)],
        ),
        compiler_params=pltpu.CompilerParams(dimension_semantics=("arbitrary",)),
        cost_estimate=pl.CostEstimate(flops=flops, bytes_accessed=bytes_accessed, transcendentals=0),
    )(dest, order, *([pieces] * per_step), w)


def ring(size, step):
    return [(i, (i + step) % size) for i in range(size)]


def per_device(tokens, norm_gain, kept_blocks, block_cols, row_counts):
    tensor_count = lax.axis_size(TP)
    heads = KVH // tensor_count * (GROUP + 2) * HD // BS
    slots = block_cols.shape[1]
    pair = lax.axis_size("ylo")
    chips = lax.axis_size("yhi")
    cores = lax.axis_size("core")
    half = lax.axis_index("ylo")
    token_count, piece_features = tokens.shape
    width = kept_blocks.shape[1]

    dest_here = jnp.where(jnp.arange(slots)[None, :] < row_counts, block_cols, heads)
    table_rows = jnp.zeros((TABLE_ROWS, width), kept_blocks.dtype)
    table_rows = table_rows.at[0, :slots].set(dest_here[0].astype(kept_blocks.dtype))
    w = lax.all_gather(jnp.concatenate([kept_blocks, table_rows], axis=0), ("x", "z"), axis=0, tiled=True)
    w = w.reshape(-1, BS + TABLE_ROWS, width)
    dest = w[:, BS, :slots].astype(jnp.int32).reshape(-1)

    floats = tokens.astype(jnp.float32)
    square_sum = lax.psum(jnp.sum(floats * floats, axis=-1), TP)
    scale = lax.rsqrt(square_sum / (piece_features * tensor_count) + 1e-05)
    normed = (floats * scale[:, None] * norm_gain.astype(jnp.float32)).astype(jnp.bfloat16)
    by_parity = normed.reshape(token_count, -1, pair, BS)
    even = by_parity[:, :, 0, :].reshape(token_count, -1)
    odd = by_parity[:, :, 1, :].reshape(token_count, -1)
    mine = jnp.where(half == 0, even, odd)
    theirs = jnp.where(half == 0, odd, even)
    partner_rows = lax.ppermute(theirs, "ylo", ring(pair, 1))
    piece = jnp.concatenate([mine, partner_rows], axis=0)

    from_below = lax.ppermute(piece, "yhi", ring(chips, 1))
    from_above = lax.ppermute(piece, "yhi", ring(chips, -1))
    cut = piece.shape[1] // 2
    far_low = lax.ppermute(from_below[:, :cut], "yhi", ring(chips, 1))
    far_high = lax.ppermute(from_above[:, cut:], "yhi", ring(chips, -1))
    far = jnp.concatenate([far_low, far_high], axis=1)
    own_core = jnp.stack([piece, from_below, from_above, far])
    other_core = lax.ppermute(own_core, "core", ring(cores, 1))
    pieces = jnp.concatenate([own_core, other_core], axis=0)

    chip = lax.axis_index("yhi")
    core = lax.axis_index("core")
    offsets = jnp.array([0, -1, 1, 2], jnp.int32)
    entry_chip = jnp.concatenate([(chip + offsets) % chips] * 2)
    entry_core = jnp.concatenate([jnp.full((4,), core), jnp.full((4,), (core + 1) % cores)])
    holder = entry_chip * cores + entry_core
    order = jnp.zeros((tensor_count,), jnp.int32).at[holder].set(jnp.arange(tensor_count, dtype=jnp.int32))

    partner_partial = block_sparse_partial(dest, order, pieces, w, 1, heads, slots, jnp.bfloat16)
    returned = lax.ppermute(partner_partial, "ylo", ring(pair, 1))
    own_partial = block_sparse_partial(dest, order, pieces, w, 0, heads, slots, jnp.float32)
    mixed = own_partial + returned.astype(jnp.float32)
    positions = jnp.arange(token_count).astype(jnp.float32)
    return rotate(mixed, positions).astype(jnp.bfloat16)


def solution(mesh):
    dp_size = mesh.shape["dp"]
    tp_size = mesh.shape["tensor"]
    fine = Mesh(mesh.devices.reshape(dp_size // 16, 8, 2, tp_size // 2, 2), DP + TP)
    spec = P(DP, TP)
    in_specs = (spec, P(TP), spec, spec, spec)
    return jax.shard_map(per_device, mesh=fine, in_specs=in_specs, out_specs=spec, check_vma=False)
```

```python
import functools

import jax
import jax.numpy as jnp
from jax import lax
from jax.experimental import pallas as pl
from jax.experimental.pallas import tpu as pltpu
from jax.sharding import Mesh
from jax.sharding import PartitionSpec as P

KVH = 8
GROUP = 8
HD = 128
BS = 128
TABLE_ROWS = 8

rope_theta = 500000.0

DP = ("x", "z", "ylo")
TP = ("yhi", "core")


def rotate(mixed, positions):
    row_count = mixed.shape[0]
    head_view = mixed.reshape(row_count, -1, GROUP + 2, HD)
    half_size = HD // 2
    inverse_freq = rope_theta ** (-(jnp.arange(half_size).astype(jnp.float32) * 2.0 / HD))
    angles = positions[:, None] * inverse_freq[None, :]
    cosine = jnp.cos(angles)[:, None, None, :]
    sine_part = jnp.sin(angles)[:, None, None, :]
    first_half = head_view[..., :half_size]
    second = head_view[..., half_size:]
    turned = jnp.concatenate(
        [first_half * cosine - second * sine_part, second * cosine + first_half * sine_part],
        axis=-1,
    )
    rotated_heads = (jnp.arange(GROUP + 2) < GROUP + 1)[None, None, :, None]
    return jnp.where(rotated_heads, turned, head_view).reshape(row_count, -1)


def partial_kernel(heads, slots, steps, rows_per_piece, per_step, dest_ref, order_ref, *refs):
    x_refs = refs[:per_step]
    w_ref, out_ref, acc_ref = refs[per_step:]
    step = pl.program_id(0)

    @pl.when(step == 0)
    def _():
        acc_ref[...] = jnp.zeros_like(acc_ref)

    for p in range(per_step):
        for j in range(rows_per_piece):
            local = p * rows_per_piece + j
            row = step * per_step * rows_per_piece + local
            features = x_refs[p][:, j * BS:(j + 1) * BS]
            for s in range(slots):
                d = dest_ref[row, s]
                acc_ref[d] += jnp.dot(
                    features, w_ref[local, :BS, s * BS:(s + 1) * BS],
                    preferred_element_type=jnp.float32,
                )

    @pl.when(step == steps - 1)
    def _():
        for c in range(heads):
            out_ref[:, c * BS:(c + 1) * BS] = acc_ref[c].astype(out_ref.dtype)


def block_sparse_partial(dest, order, pieces, w, token_half, heads, slots, out_dtype):
    count, both, piece_features = pieces.shape
    tokens = both // 2
    rows_per_piece = piece_features // BS
    per_step = 4 if count % 4 == 0 else 1
    steps = count // per_step
    kernel = functools.partial(partial_kernel, heads, slots, steps, rows_per_piece, per_step)
    flops = 2 * tokens * count * piece_features * slots * BS
    bytes_accessed = (tokens * count * piece_features * 2 + w.size * 2
                      + tokens * heads * BS * jnp.dtype(out_dtype).itemsize)

    def piece_map(p):
        return lambda i, d, o: (o[i * per_step + p], token_half, 0)

    return pl.pallas_call(
        kernel,
        out_shape=jax.ShapeDtypeStruct((tokens, heads * BS), out_dtype),
        grid_spec=pltpu.PrefetchScalarGridSpec(
            num_scalar_prefetch=2,
            grid=(steps,),
            in_specs=[pl.BlockSpec((None, tokens, piece_features), piece_map(p)) for p in range(per_step)]
            + [pl.BlockSpec((per_step * rows_per_piece, w.shape[1], slots * BS), lambda i, d, o: (i, 0, 0))],
            out_specs=pl.BlockSpec((tokens, heads * BS), lambda i, d, o: (0, 0)),
            scratch_shapes=[pltpu.VMEM((heads + 1, tokens, BS), jnp.float32)],
        ),
        compiler_params=pltpu.CompilerParams(dimension_semantics=("arbitrary",)),
        cost_estimate=pl.CostEstimate(flops=flops, bytes_accessed=bytes_accessed, transcendentals=0),
    )(dest, order, *([pieces] * per_step), w)


def ring(size, step):
    return [(i, (i + step) % size) for i in range(size)]


def per_device(tokens, norm_gain, kept_blocks, block_cols, row_counts):
    tensor_count = lax.axis_size(TP)
    heads = KVH // tensor_count * (GROUP + 2) * HD // BS
    slots = block_cols.shape[1]
    pair = lax.axis_size("ylo")
    chips = lax.axis_size("yhi")
    cores = lax.axis_size("core")
    half = lax.axis_index("ylo")
    token_count, piece_features = tokens.shape
    width = kept_blocks.shape[1]

    dest_here = jnp.where(jnp.arange(slots)[None, :] < row_counts, block_cols, heads)
    table_rows = jnp.zeros((TABLE_ROWS, width), kept_blocks.dtype)
    table_rows = table_rows.at[0, :slots].set(dest_here[0].astype(kept_blocks.dtype))
    w = lax.all_gather(jnp.concatenate([kept_blocks, table_rows], axis=0), ("x", "z"), axis=0, tiled=True)
    w = w.reshape(-1, BS + TABLE_ROWS, width)
    dest = w[:, BS, :slots].astype(jnp.int32)

    floats = tokens.astype(jnp.float32)
    square_sum = lax.psum(jnp.sum(floats * floats, axis=-1), TP)
    scale = lax.rsqrt(square_sum / (piece_features * tensor_count) + 1e-05)
    normed = (floats * scale[:, None] * norm_gain.astype(jnp.float32)).astype(jnp.bfloat16)
    by_parity = normed.reshape(token_count, -1, pair, BS)
    even = by_parity[:, :, 0, :].reshape(token_count, -1)
    odd = by_parity[:, :, 1, :].reshape(token_count, -1)
    mine = jnp.where(half == 0, even, odd)
    theirs = jnp.where(half == 0, odd, even)
    partner_rows = lax.ppermute(theirs, "ylo", ring(pair, 1))
    piece = jnp.concatenate([mine, partner_rows], axis=0)

    from_below = lax.ppermute(piece, "yhi", ring(chips, 1))
    from_above = lax.ppermute(piece, "yhi", ring(chips, -1))
    cut = piece.shape[1] // 2
    far_low = lax.ppermute(from_below[:, :cut], "yhi", ring(chips, 1))
    far_high = lax.ppermute(from_above[:, cut:], "yhi", ring(chips, -1))
    far = jnp.concatenate([far_low, far_high], axis=1)
    own_core = jnp.stack([piece, from_below, from_above, far])
    other_core = lax.ppermute(own_core, "core", ring(cores, 1))
    pieces = jnp.concatenate([own_core, other_core], axis=0)

    chip = lax.axis_index("yhi")
    core = lax.axis_index("core")
    offsets = jnp.array([0, -1, 1, 2], jnp.int32)
    entry_chip = jnp.concatenate([(chip + offsets) % chips] * 2)
    entry_core = jnp.concatenate([jnp.full((4,), core), jnp.full((4,), (core + 1) % cores)])
    holder = entry_chip * cores + entry_core
    order = jnp.zeros((tensor_count,), jnp.int32).at[holder].set(jnp.arange(tensor_count, dtype=jnp.int32))

    partner_partial = block_sparse_partial(dest, order, pieces, w, 1, heads, slots, jnp.bfloat16)
    returned = lax.ppermute(partner_partial, "ylo", ring(pair, 1))
    own_partial = block_sparse_partial(dest, order, pieces, w, 0, heads, slots, jnp.float32)
    mixed = own_partial + returned.astype(jnp.float32)
    positions = jnp.arange(token_count).astype(jnp.float32)
    return rotate(mixed, positions).astype(jnp.bfloat16)


def solution(mesh):
    dp_size = mesh.shape["dp"]
    tp_size = mesh.shape["tensor"]
    fine = Mesh(mesh.devices.reshape(dp_size // 16, 8, 2, tp_size // 2, 2), DP + TP)
    spec = P(DP, TP)
    in_specs = (spec, P(TP), spec, spec, spec)
    return jax.shard_map(per_device, mesh=fine, in_specs=in_specs, out_specs=spec, check_vma=False)
```
